32 devices in a mesh: groups: 2 (over x), dp: 4 (over y, core), hidden: 4 (over z).
Axes of the slice: x: 2, y: 2, z: 4, core: 2. Of those that a mesh axis runs over, the one named last changes fastest.
Arguments:
- activations: bfloat16 [24576, 8192], P(('groups', 'dp'), 'hidden'), parts along dimension 0, may hold values from -6 to 6
- cotangent: bfloat16 [24576, 8192], P(('groups', 'dp'), 'hidden'), parts along dimension 0
- up_factor_matrix: bfloat16 [8192, 64], P('hidden'), may hold values from -0.0625 to 0.0625
- input_sketch: bfloat16 [8192, 128], P('hidden'), may hold values from -0.0625 to 0.0625
- rank_sketch: float32 [64, 32], replicated, may hold values from -0.75 to 0.75
Outputs:
- features: bfloat16 [48, 4096], P(('groups', 'dp'), 'hidden'), parts along dimension 0
- scores: float32 [48, 24], P(('groups', 'dp'), 'hidden'), parts along dimension 0
The draws below stay inside these ranges and needn't reach their ends.
There are 2 independent parts, one for each index of `groups`. The reference program is written for one: setup_inputs(seed, part) draws one part's arguments, and reference() takes and returns one part's arrays. A program takes and returns all parts, laid end to end along the dimension named above; an argument that names none is the same for every part. Nothing has to cross between parts.
All inputs are finite; a program needn't handle non-finite values.
Results may differ from the reference program's by a relative error of at most 0.0017.
Values may be sent and summed in bfloat16 or wider, within the bound.
No kernel may reach another device: no remote copies, remote signals or barrier semaphores. Data moves between devices by JAX's collectives and lax.ppermute only.
A program may use at most 64 MiB of HBM per device.

```python
import math
import jax
import jax.numpy as jnp
from jax import lax

D_IN = 8192
OUTPUT_WIDTH = 8192
LOW_RANK = 64
K_R = 32
K_IN = 128
FEAT = 4096
SEQ = 512
N_EX = 24


def draw_cotangent(key, part):
    key_ex, key_tok, key_base = jax.random.split(key, 3)
    ex_index = jnp.arange(N_EX, dtype=jnp.float32)
    trend = 3.0 ** (ex_index / max(N_EX - 1, 1))
    example_scale = trend * jnp.exp(jax.random.uniform(key_ex, (N_EX,), minval=-0.5, maxval=0.5))
    tok_scale = jnp.exp(jax.random.uniform(key_tok, (N_EX * SEQ,), minval=0.0, maxval=2.3))
    row_scale = jnp.repeat(example_scale, SEQ) * tok_scale
    base_values = jax.random.normal(key_base, (N_EX * SEQ, OUTPUT_WIDTH))
    return (base_values * row_scale[:, None] * 0.2).astype(jnp.bfloat16)


def level_of(stream_key, dims, shards, smallest, high):
    def one(position, blocks):
        steps = jax.random.uniform(jax.random.fold_in(jax.random.fold_in(stream_key, 6), position), (blocks,), jnp.float32, smallest / len(shards), high / len(shards))
        return jnp.repeat(jnp.exp(steps), dims[position] // blocks).reshape((-1,) + (1,) * (len(dims) - position - 1))

    factor_of = one(*shards[0])
    for cut in shards[1:]:
        factor_of = factor_of * one(*cut)
    return factor_of


def bell_draw(key, extent, deviation, reach, cuts=(), kind=jnp.bfloat16):
    result = deviation * jax.random.normal(key, extent, jnp.float32)
    if cuts:
        result = result * level_of(key, extent, cuts, -0.22, 0.18)
    return jnp.clip(result, -reach, reach).astype(kind)


def setup_inputs(seed: int = 0, part: int = 0) -> dict:
    seeds = jax.random.split(jax.random.key(seed), 6)
    part_keys = jax.random.split(jax.random.fold_in(seeds[5], part), 6)
    return {
        "activations": bell_draw(part_keys[0], (N_EX * SEQ, D_IN), 1.0, 6.0, ((0, 4), (1, 4))),
        "cotangent": draw_cotangent(jax.random.fold_in(jax.random.fold_in(seeds[5], part), 71), part),
        "up_factor_matrix": bell_draw(seeds[2], (OUTPUT_WIDTH, LOW_RANK), OUTPUT_WIDTH ** -0.5, 0.0625, ((0, 4),)),
        "input_sketch": bell_draw(seeds[3], (D_IN, K_IN), D_IN ** -0.5, 0.0625, ((0, 4),)),
        "rank_sketch": bell_draw(seeds[4], (LOW_RANK, K_R), LOW_RANK ** -0.5, 0.75, (), jnp.float32),
    }


epsilon = 1e-05

def reference(activations, cotangent, up_factor_matrix, input_sketch, rank_sketch):
    backward_pass = jnp.dot(cotangent, up_factor_matrix, preferred_element_type=jnp.float32)
    rank_side = jnp.dot(backward_pass, rank_sketch, precision=lax.Precision.HIGHEST)
    input_side = jnp.dot(activations, input_sketch, preferred_element_type=jnp.float32)
    rank_side = rank_side.reshape(N_EX, SEQ, K_R)
    input_side = input_side.reshape(N_EX, SEQ, K_IN)
    outer = jnp.einsum('esa,esb->eab', rank_side, input_side, precision=lax.Precision.HIGHEST)
    features = outer.reshape(N_EX, FEAT).astype(jnp.bfloat16)
    widened = features.astype(jnp.float32)
    weight = 1.0 / (lax.optimization_barrier(jnp.sum(widened * widened, axis=0)) / N_EX + epsilon)
    scores = jnp.dot(widened * weight, widened.T, precision=lax.Precision.HIGHEST) / math.sqrt(FEAT)
    return (features, scores)
```

```python
import math

import jax
import jax.numpy as jnp
from jax import lax
from jax.sharding import PartitionSpec as P

SEQ = 512
epsilon = 1e-05
HI = lax.Precision.HIGHEST


def partial_features(activations, cotangent, up_factor_matrix, input_sketch, rank_sketch):
    examples = activations.shape[0] // SEQ
    backward_pass = jnp.dot(cotangent, up_factor_matrix, preferred_element_type=jnp.float32)
    rank_part = jnp.dot(backward_pass, rank_sketch, precision=HI)
    rank_full = lax.psum(rank_part, "hidden")
    input_part = jnp.dot(activations, input_sketch, preferred_element_type=jnp.float32)
    rank_rows = rank_full.reshape(examples, SEQ, rank_full.shape[1])
    input_rows = input_part.reshape(examples, SEQ, input_part.shape[1])
    return jnp.einsum("esa,esb->eab", rank_rows, input_rows, precision=HI)


def per_device(activations, cotangent, up_factor_matrix, input_sketch, rank_sketch):
    examples = activations.shape[0] // SEQ
    partial = partial_features(activations, cotangent, up_factor_matrix, input_sketch, rank_sketch)
    own = lax.psum_scatter(partial, "hidden", scatter_dimension=1, tiled=True)
    features = own.reshape(examples, -1).astype(jnp.bfloat16)
    widened = features.astype(jnp.float32)
    every = lax.all_gather(features, "dp", axis=0, tiled=True).astype(jnp.float32)
    all_count = every.shape[0]
    weight = 1.0 / (jnp.sum(every * every, axis=0) / all_count + epsilon)
    partial_scores = jnp.dot(widened * weight, every.T, precision=HI)
    feat_total = features.shape[1] * lax.axis_size("hidden")
    scores = lax.psum_scatter(partial_scores / math.sqrt(feat_total), "hidden", scatter_dimension=1, tiled=True)
    return (features, scores)


def solution(mesh):
    placed = (
        P(("groups", "dp"), "hidden"),
        P(("groups", "dp"), "hidden"),
        P("hidden", None),
        P("hidden", None),
        P(),
    )
    return jax.shard_map(
        per_device,
        mesh=mesh,
        in_specs=placed,
        out_specs=(P(("groups", "dp"), "hidden"), P(("groups", "dp"), "hidden")),
        check_vma=False,
    )
```

```python
import math

import jax
import jax.numpy as jnp
from jax import lax
from jax.sharding import PartitionSpec as P

SEQ = 512
epsilon = 1e-05
HI = lax.Precision.HIGHEST


def exchange(blocks, axis):
    n = lax.axis_size(axis)
    me = lax.axis_index(axis)
    got = [lax.dynamic_index_in_dim(blocks, me, 0, keepdims=False)]
    for d in range(1, n):
        piece = lax.dynamic_index_in_dim(blocks, (me + d) % n, 0, keepdims=False)
        got.append(lax.ppermute(piece, axis, [(i, (i + d) % n) for i in range(n)]))
    return got


def reduce_scatter(blocks, axis):
    got = exchange(blocks, axis)
    acc = got[0]
    for g in got[1:]:
        acc = acc + g
    return acc


def all_gather(x, axis):
    n = lax.axis_size(axis)
    me = lax.axis_index(axis)
    out = jnp.zeros((n,) + x.shape, x.dtype)
    out = lax.dynamic_update_index_in_dim(out, x, me, 0)
    for d in range(1, n):
        got = lax.ppermute(x, axis, [(i, (i + d) % n) for i in range(n)])
        out = lax.dynamic_update_index_in_dim(out, got, (me - d) % n, 0)
    return out


def all_reduce(x, axis):
    n = lax.axis_size(axis)
    acc = reduce_scatter(x.reshape((n, -1) + x.shape[1:]), axis)
    return all_gather(acc, axis).reshape(x.shape)


def per_device(activations, cotangent, up_factor_matrix, input_sketch, rank_sketch):
    shards = lax.axis_size("hidden")
    examples = activations.shape[0] // SEQ
    backward_pass = jnp.dot(cotangent, up_factor_matrix, preferred_element_type=jnp.float32)
    rank_part = jnp.dot(backward_pass, rank_sketch, precision=HI)
    rank_full = all_reduce(rank_part, "hidden")
    input_part = jnp.dot(activations, input_sketch, preferred_element_type=jnp.float32)
    rank_rows = rank_full.reshape(examples, SEQ, rank_full.shape[1])
    input_rows = input_part.reshape(examples, SEQ, input_part.shape[1])
    partial = jnp.einsum("esa,esb->eab", rank_rows, input_rows, precision=HI)
    own_a = partial.shape[1] // shards
    blocks = partial.reshape(examples, shards, own_a, -1).transpose(1, 0, 2, 3)
    own = reduce_scatter(blocks, "hidden")
    features = own.reshape(examples, -1).astype(jnp.bfloat16)
    widened = features.astype(jnp.float32)
    every = all_gather(features, "dp").reshape(-1, features.shape[1]).astype(jnp.float32)
    all_count = every.shape[0]
    weight = 1.0 / (jnp.sum(every * every, axis=0) / all_count + epsilon)
    partial_scores = jnp.dot(widened * weight, every.T, precision=HI)
    feat_total = features.shape[1] * shards
    score_blocks = partial_scores.reshape(examples, shards, -1).transpose(1, 0, 2)
    scores = reduce_scatter(score_blocks, "hidden") / math.sqrt(feat_total)
    return (features, scores)


def solution(mesh):
    placed = (
        P(("groups", "dp"), "hidden"),
        P(("groups", "dp"), "hidden"),
        P("hidden", None),
        P("hidden", None),
        P(),
    )
    return jax.shard_map(
        per_device,
        mesh=mesh,
        in_specs=placed,
        out_specs=(P(("groups", "dp"), "hidden"), P(("groups", "dp"), "hidden")),
        check_vma=False,
    )
```

```python
import math

import jax
import jax.numpy as jnp
from jax import lax
from jax.sharding import PartitionSpec as P

SEQ = 512
epsilon = 1e-05
HI = lax.Precision.HIGHEST


def exchange(blocks, axis):
    n = lax.axis_size(axis)
    me = lax.axis_index(axis)
    got = [lax.dynamic_index_in_dim(blocks, me, 0, keepdims=False)]
    for d in range(1, n):
        piece = lax.dynamic_index_in_dim(blocks, (me + d) % n, 0, keepdims=False)
        got.append(lax.ppermute(piece, axis, [(i, (i + d) % n) for i in range(n)]))
    return got


def reduce_scatter(blocks, axis):
    got = exchange(blocks, axis)
    acc = got[0]
    for g in got[1:]:
        acc = acc + g
    return acc


def all_gather(x, axis):
    n = lax.axis_size(axis)
    me = lax.axis_index(axis)
    out = jnp.zeros((n,) + x.shape, x.dtype)
    out = lax.dynamic_update_index_in_dim(out, x, me, 0)
    for d in range(1, n):
        got = lax.ppermute(x, axis, [(i, (i + d) % n) for i in range(n)])
        out = lax.dynamic_update_index_in_dim(out, got, (me - d) % n, 0)
    return out


def all_reduce(x, axis):
    n = lax.axis_size(axis)
    acc = reduce_scatter(x.reshape((n, -1) + x.shape[1:]), axis)
    return all_gather(acc, axis).reshape(x.shape)


def per_device(activations, cotangent, up_factor_matrix, input_sketch, rank_sketch):
    shards = lax.axis_size("hidden")
    me = lax.axis_index("hidden")
    examples = activations.shape[0] // SEQ
    backward_t = lax.dot_general(up_factor_matrix, cotangent, (((0,), (1,)), ((), ())),
                                 preferred_element_type=jnp.float32)
    rank_t = lax.dot_general(rank_sketch, backward_t, (((0,), (0,)), ((), ())), precision=HI)
    own_a = rank_t.shape[0] // shards
    rank_own = reduce_scatter(rank_t.reshape(shards, own_a, -1), "hidden")
    input_part = jnp.dot(activations, input_sketch, preferred_element_type=jnp.float32)
    input_rows = input_part.reshape(examples, SEQ, input_part.shape[1])

    def outer(rank_block):
        rows = rank_block.reshape(own_a, examples, SEQ)
        return jnp.einsum("aes,esb->eab", rows, input_rows, precision=HI)

    own = outer(rank_own)
    for d in range(1, shards):
        visiting = lax.ppermute(rank_own, "hidden", [(i, (i + d) % shards) for i in range(shards)])
        back = [(i, (i - d) % shards) for i in range(shards)]
        own = own + lax.ppermute(outer(visiting), "hidden", back)
    features = own.reshape(examples, -1).astype(jnp.bfloat16)
    widened = features.astype(jnp.float32)
    every = all_gather(features, "dp").reshape(-1, features.shape[1]).astype(jnp.float32)
    all_count = every.shape[0]
    weight = 1.0 / (jnp.sum(every * every, axis=0) / all_count + epsilon)
    partial_scores = jnp.dot(widened * weight, every.T, precision=HI)
    feat_total = features.shape[1] * shards
    score_blocks = partial_scores.reshape(examples, shards, -1).transpose(1, 0, 2)
    scores = reduce_scatter(score_blocks, "hidden") / math.sqrt(feat_total)
    return (features, scores)


def solution(mesh):
    placed = (
        P(("groups", "dp"), "hidden"),
        P(("groups", "dp"), "hidden"),
        P("hidden", None),
        P("hidden", None),
        P(),
    )
    return jax.shard_map(
        per_device,
        mesh=mesh,
        in_specs=placed,
        out_specs=(P(("groups", "dp"), "hidden"), P(("groups", "dp"), "hidden")),
        check_vma=False,
    )
```

```python
import math

import jax
import jax.numpy as jnp
from jax import lax
from jax.sharding import PartitionSpec as P

SEQ = 512
epsilon = 1e-05
HI = lax.Precision.HIGHEST


from jax.experimental import pallas as pl
from jax.experimental.pallas import tpu as pltpu

ROWS = 512


def _split(x):
    hi = x.astype(jnp.bfloat16)
    return hi, (x - hi.astype(jnp.float32)).astype(jnp.bfloat16)


def _rank_kernel(cot_ref, bt_ref, srt_ref, out_ref):
    back_t = lax.dot_general(bt_ref[...], cot_ref[...], (((1,), (1,)), ((), ())),
                             preferred_element_type=jnp.float32)
    b_hi, b_lo = _split(back_t)
    s_hi, s_lo = _split(srt_ref[...])
    f32 = jnp.float32
    out = jnp.dot(s_hi, b_hi, preferred_element_type=f32)
    out = out + jnp.dot(s_hi, b_lo, preferred_element_type=f32)
    out = out + jnp.dot(s_lo, b_hi, preferred_element_type=f32)
    out_ref[...] = out


def rank_side_t(cotangent, up_factor_matrix, rank_sketch, interpret=False):
    tokens, width = cotangent.shape
    low = up_factor_matrix.shape[1]
    k_r = rank_sketch.shape[1]
    return pl.pallas_call(
        _rank_kernel,
        grid=(tokens // ROWS,),
        in_specs=[
            pl.BlockSpec((ROWS, width), lambda i: (i, 0)),
            pl.BlockSpec((low, width), lambda i: (0, 0)),
            pl.BlockSpec((k_r, low), lambda i: (0, 0)),
        ],
        out_specs=pl.BlockSpec((k_r, ROWS), lambda i: (0, i)),
        out_shape=jax.ShapeDtypeStruct((k_r, tokens), jnp.float32),
        cost_estimate=pl.CostEstimate(flops=2 * tokens * width * low, transcendentals=0,
                                      bytes_accessed=2 * tokens * width + 4 * tokens * k_r),
        interpret=interpret,
    )(cotangent, up_factor_matrix.T, rank_sketch.T)


def _input_kernel(act_ref, s_ref, out_ref):
    out_ref[...] = jnp.dot(act_ref[...], s_ref[...], preferred_element_type=jnp.float32)


def input_side(activations, input_sketch, interpret=False):
    tokens, width = activations.shape
    k_in = input_sketch.shape[1]
    return pl.pallas_call(
        _input_kernel,
        grid=(tokens // ROWS,),
        in_specs=[
            pl.BlockSpec((ROWS, width), lambda i: (i, 0)),
            pl.BlockSpec((width, k_in), lambda i: (0, 0)),
        ],
        out_specs=pl.BlockSpec((ROWS, k_in), lambda i: (i, 0)),
        out_shape=jax.ShapeDtypeStruct((tokens, k_in), jnp.float32),
        cost_estimate=pl.CostEstimate(flops=2 * tokens * width * k_in, transcendentals=0,
                                      bytes_accessed=2 * tokens * width + 4 * tokens * k_in),
        interpret=interpret,
    )(activations, input_sketch)


def exchange(blocks, axis):
    n = lax.axis_size(axis)
    me = lax.axis_index(axis)
    got = [lax.dynamic_index_in_dim(blocks, me, 0, keepdims=False)]
    for d in range(1, n):
        piece = lax.dynamic_index_in_dim(blocks, (me + d) % n, 0, keepdims=False)
        got.append(lax.ppermute(piece, axis, [(i, (i + d) % n) for i in range(n)]))
    return got


def reduce_scatter(blocks, axis):
    got = exchange(blocks, axis)
    acc = got[0]
    for g in got[1:]:
        acc = acc + g
    return acc


def all_gather(x, axis):
    n = lax.axis_size(axis)
    me = lax.axis_index(axis)
    out = jnp.zeros((n,) + x.shape, x.dtype)
    out = lax.dynamic_update_index_in_dim(out, x, me, 0)
    for d in range(1, n):
        got = lax.ppermute(x, axis, [(i, (i + d) % n) for i in range(n)])
        out = lax.dynamic_update_index_in_dim(out, got, (me - d) % n, 0)
    return out


def all_reduce(x, axis):
    n = lax.axis_size(axis)
    acc = reduce_scatter(x.reshape((n, -1) + x.shape[1:]), axis)
    return all_gather(acc, axis).reshape(x.shape)


def per_device(activations, cotangent, up_factor_matrix, input_sketch, rank_sketch):
    shards = lax.axis_size("hidden")
    me = lax.axis_index("hidden")
    examples = activations.shape[0] // SEQ
    rank_t = rank_side_t(cotangent, up_factor_matrix, rank_sketch)
    own_a = rank_t.shape[0] // shards
    rank_own = reduce_scatter(rank_t.reshape(shards, own_a, -1), "hidden")
    input_part = input_side(activations, input_sketch)
    input_rows = input_part.reshape(examples, SEQ, input_part.shape[1])

    def outer(rank_block):
        rows = rank_block.reshape(own_a, examples, SEQ)
        return jnp.einsum("aes,esb->eab", rows, input_rows, precision=HI)

    own = outer(rank_own)
    for d in range(1, shards):
        visiting = lax.ppermute(rank_own, "hidden", [(i, (i + d) % shards) for i in range(shards)])
        back = [(i, (i - d) % shards) for i in range(shards)]
        own = own + lax.ppermute(outer(visiting), "hidden", back)
    features = own.reshape(examples, -1).astype(jnp.bfloat16)
    widened = features.astype(jnp.float32)
    every = all_gather(features, "dp").reshape(-1, features.shape[1]).astype(jnp.float32)
    all_count = every.shape[0]
    weight = 1.0 / (jnp.sum(every * every, axis=0) / all_count + epsilon)
    partial_scores = jnp.dot(widened * weight, every.T, precision=HI)
    feat_total = features.shape[1] * shards
    score_blocks = partial_scores.reshape(examples, shards, -1).transpose(1, 0, 2)
    scores = reduce_scatter(score_blocks, "hidden") / math.sqrt(feat_total)
    return (features, scores)


def solution(mesh):
    placed = (
        P(("groups", "dp"), "hidden"),
        P(("groups", "dp"), "hidden"),
        P("hidden", None),
        P("hidden", None),
        P(),
    )
    return jax.shard_map(
        per_device,
        mesh=mesh,
        in_specs=placed,
        out_specs=(P(("groups", "dp"), "hidden"), P(("groups", "dp"), "hidden")),
        check_vma=False,
    )
```

```python
import math

import jax
import jax.numpy as jnp
from jax import lax
from jax.sharding import PartitionSpec as P

SEQ = 512
epsilon = 1e-05
HI = lax.Precision.HIGHEST


def exchange(blocks, axis):
    n = lax.axis_size(axis)
    me = lax.axis_index(axis)
    got = [lax.dynamic_index_in_dim(blocks, me, 0, keepdims=False)]
    for d in range(1, n):
        piece = lax.dynamic_index_in_dim(blocks, (me + d) % n, 0, keepdims=False)
        got.append(lax.ppermute(piece, axis, [(i, (i + d) % n) for i in range(n)]))
    return got


def _bits(n):
    k = n.bit_length() - 1
    return k if n == 1 << k else None


def _swap(x, axis, bit):
    n = lax.axis_size(axis)
    return lax.ppermute(x, axis, [(i, i ^ (1 << bit)) for i in range(n)])


def reduce_scatter(blocks, axis):
    n = lax.axis_size(axis)
    k = _bits(n)
    if k is None:
        got = exchange(blocks, axis)
        acc = got[0]
        for g in got[1:]:
            acc = acc + g
        return acc
    me = lax.axis_index(axis)
    cur = blocks.reshape((2,) * k + blocks.shape[1:])
    for bit in range(k):
        dim = k - 1 - bit
        mine = (me >> bit) & 1
        keep = lax.dynamic_index_in_dim(cur, mine, dim, keepdims=False)
        give = lax.dynamic_index_in_dim(cur, 1 - mine, dim, keepdims=False)
        cur = keep + _swap(give, axis, bit)
    return cur


def all_gather(x, axis):
    n = lax.axis_size(axis)
    me = lax.axis_index(axis)
    k = _bits(n)
    if k is None:
        out = jnp.zeros((n,) + x.shape, x.dtype)
        out = lax.dynamic_update_index_in_dim(out, x, me, 0)
        for d in range(1, n):
            got = lax.ppermute(x, axis, [(i, (i + d) % n) for i in range(n)])
            out = lax.dynamic_update_index_in_dim(out, got, (me - d) % n, 0)
        return out
    cur = x
    for step, bit in enumerate(reversed(range(k))):
        other = _swap(cur, axis, bit)
        low = ((me >> bit) & 1) == 0
        cur = jnp.stack([jnp.where(low, cur, other), jnp.where(low, other, cur)], axis=step)
    return cur.reshape((n,) + x.shape)


def per_device(activations, cotangent, up_factor_matrix, input_sketch, rank_sketch):
    shards = lax.axis_size("hidden")
    me = lax.axis_index("hidden")
    examples = activations.shape[0] // SEQ
    backward_t = lax.dot_general(up_factor_matrix, cotangent, (((0,), (1,)), ((), ())),
                                 preferred_element_type=jnp.float32)
    rank_t = lax.dot_general(rank_sketch, backward_t, (((0,), (0,)), ((), ())), precision=HI)
    own_a = rank_t.shape[0] // shards
    rank_own = reduce_scatter(rank_t.reshape(shards, own_a, -1), "hidden")
    input_part = jnp.dot(activations, input_sketch, preferred_element_type=jnp.float32)
    input_rows = input_part.reshape(examples, SEQ, input_part.shape[1])

    def outer(rank_block):
        rows = rank_block.reshape(rank_block.shape[0], examples, SEQ)
        return jnp.einsum("aes,esb->eab", rows, input_rows, precision=HI)

    rank_full = all_gather(rank_own, "hidden").reshape(rank_t.shape)
    partial = outer(rank_full)
    own = reduce_scatter(partial.reshape(examples, shards, own_a, -1).transpose(1, 0, 2, 3), "hidden")
    features = own.reshape(examples, -1).astype(jnp.bfloat16)
    widened = features.astype(jnp.float32)
    every = all_gather(features, "dp").reshape(-1, features.shape[1]).astype(jnp.float32)
    all_count = every.shape[0]
    weight = 1.0 / (jnp.sum(every * every, axis=0) / all_count + epsilon)
    partial_scores = jnp.dot(widened * weight, every.T, precision=HI)
    feat_total = features.shape[1] * shards
    score_blocks = partial_scores.reshape(examples, shards, -1).transpose(1, 0, 2)
    scores = reduce_scatter(score_blocks, "hidden") / math.sqrt(feat_total)
    return (features, scores)


def solution(mesh):
    placed = (
        P(("groups", "dp"), "hidden"),
        P(("groups", "dp"), "hidden"),
        P("hidden", None),
        P("hidden", None),
        P(),
    )
    return jax.shard_map(
        per_device,
        mesh=mesh,
        in_specs=placed,
        out_specs=(P(("groups", "dp"), "hidden"), P(("groups", "dp"), "hidden")),
        check_vma=False,
    )
```

```python
import math

import jax
import jax.numpy as jnp
from jax import lax
from jax.sharding import PartitionSpec as P


SEQ = 512
epsilon = 1e-05
HI = lax.Precision.HIGHEST


def exchange(blocks, axis):
    n = lax.axis_size(axis)
    me = lax.axis_index(axis)
    got = [lax.dynamic_index_in_dim(blocks, me, 0, keepdims=False)]
    for d in range(1, n):
        piece = lax.dynamic_index_in_dim(blocks, (me + d) % n, 0, keepdims=False)
        got.append(lax.ppermute(piece, axis, [(i, (i + d) % n) for i in range(n)]))
    return got


def reduce_scatter(blocks, axis):
    got = exchange(blocks, axis)
    acc = got[0]
    for g in got[1:]:
        acc = acc + g
    return acc


def all_gather(x, axis):
    n = lax.axis_size(axis)
    me = lax.axis_index(axis)
    out = jnp.zeros((n,) + x.shape, x.dtype)
    out = lax.dynamic_update_index_in_dim(out, x, me, 0)
    for d in range(1, n):
        got = lax.ppermute(x, axis, [(i, (i + d) % n) for i in range(n)])
        out = lax.dynamic_update_index_in_dim(out, got, (me - d) % n, 0)
    return out


def body(activations, cotangent, up_factor_matrix, input_sketch, rank_sketch):
    shards = lax.axis_size("hidden")
    examples = activations.shape[0] // SEQ
    backward_t = lax.dot_general(up_factor_matrix, cotangent, (((0,), (1,)), ((), ())),
                                 preferred_element_type=jnp.float32)
    rank_t = lax.dot_general(rank_sketch, backward_t, (((0,), (0,)), ((), ())), precision=HI)
    own_a = rank_t.shape[0] // shards
    rank_own = reduce_scatter(rank_t.reshape(shards, own_a, -1), "hidden")
    input_part = jnp.dot(activations, input_sketch, preferred_element_type=jnp.float32)
    input_rows = input_part.reshape(examples, SEQ, input_part.shape[1])

    def outer(rank_block):
        rows = rank_block.reshape(own_a, examples, SEQ)
        return jnp.einsum("aes,esb->eab", rows, input_rows, precision=HI)

    own = outer(rank_own)
    for d in range(1, shards):
        visiting = lax.ppermute(rank_own, "hidden", [(i, (i + d) % shards) for i in range(shards)])
        back = [(i, (i - d) % shards) for i in range(shards)]
        own = own + lax.ppermute(outer(visiting), "hidden", back)
    features = own.reshape(examples, -1).astype(jnp.bfloat16)
    widened = features.astype(jnp.float32)
    every = all_gather(features, "dp").reshape(-1, features.shape[1]).astype(jnp.float32)
    all_count = every.shape[0]
    weight = 1.0 / (jnp.sum(every * every, axis=0) / all_count + epsilon)
    partial_scores = jnp.dot(widened * weight, every.T, precision=HI)
    feat_total = features.shape[1] * shards
    score_blocks = partial_scores.reshape(examples, shards, -1).transpose(1, 0, 2)
    scores = reduce_scatter(score_blocks, "hidden") / math.sqrt(feat_total)
    return (features, scores)


def solution(mesh):
    placed = (
        P(("groups", "dp"), "hidden"),
        P(("groups", "dp"), "hidden"),
        P("hidden", None),
        P("hidden", None),
        P(),
    )
    return jax.shard_map(
        body,
        mesh=mesh,
        in_specs=placed,
        out_specs=(P(("groups", "dp"), "hidden"), P(("groups", "dp"), "hidden")),
        check_vma=False,
    )
```

```python
import math

import jax
import jax.numpy as jnp
from jax import lax
from jax.sharding import PartitionSpec as P


SEQ = 512
epsilon = 1e-05
HI = lax.Precision.HIGHEST


def exchange(blocks, axis):
    n = lax.axis_size(axis)
    me = lax.axis_index(axis)
    got = [lax.dynamic_index_in_dim(blocks, me, 0, keepdims=False)]
    for d in range(1, n):
        piece = lax.dynamic_index_in_dim(blocks, (me + d) % n, 0, keepdims=False)
        got.append(lax.ppermute(piece, axis, [(i, (i + d) % n) for i in range(n)]))
    return got


def reduce_scatter(blocks, axis):
    got = exchange(blocks, axis)
    acc = got[0]
    for g in got[1:]:
        acc = acc + g
    return acc


def all_gather(x, axis):
    n = lax.axis_size(axis)
    me = lax.axis_index(axis)
    out = jnp.zeros((n,) + x.shape, x.dtype)
    out = lax.dynamic_update_index_in_dim(out, x, me, 0)
    for d in range(1, n):
        got = lax.ppermute(x, axis, [(i, (i + d) % n) for i in range(n)])
        out = lax.dynamic_update_index_in_dim(out, got, (me - d) % n, 0)
    return out


def body(activations, cotangent, up_factor_matrix, input_sketch, rank_sketch):
    shards = lax.axis_size("hidden")
    examples = activations.shape[0] // SEQ
    backward_pass = jnp.dot(cotangent, up_factor_matrix, preferred_element_type=jnp.float32)
    rank_t = jnp.dot(backward_pass, rank_sketch, precision=HI).T
    own_a = rank_t.shape[0] // shards
    rank_own = reduce_scatter(rank_t.reshape(shards, own_a, -1), "hidden")
    input_part = jnp.dot(activations, input_sketch, preferred_element_type=jnp.float32)
    input_rows = input_part.reshape(examples, SEQ, input_part.shape[1])

    def outer(rank_block):
        rows = rank_block.reshape(own_a, examples, SEQ)
        return jnp.einsum("aes,esb->eab", rows, input_rows, precision=HI)

    own = outer(rank_own)
    for d in range(1, shards):
        visiting = lax.ppermute(rank_own, "hidden", [(i, (i + d) % shards) for i in range(shards)])
        back = [(i, (i - d) % shards) for i in range(shards)]
        own = own + lax.ppermute(outer(visiting), "hidden", back)
    features = own.reshape(examples, -1).astype(jnp.bfloat16)
    widened = features.astype(jnp.float32)
    every = all_gather(features, "dp").reshape(-1, features.shape[1]).astype(jnp.float32)
    all_count = every.shape[0]
    weight = 1.0 / (jnp.sum(every * every, axis=0) / all_count + epsilon)
    partial_scores = jnp.dot(widened * weight, every.T, precision=HI)
    feat_total = features.shape[1] * shards
    score_blocks = partial_scores.reshape(examples, shards, -1).transpose(1, 0, 2)
    scores = reduce_scatter(score_blocks, "hidden") / math.sqrt(feat_total)
    return (features, scores)


def solution(mesh):
    placed = (
        P(("groups", "dp"), "hidden"),
        P(("groups", "dp"), "hidden"),
        P("hidden", None),
        P("hidden", None),
        P(),
    )
    return jax.shard_map(
        body,
        mesh=mesh,
        in_specs=placed,
        out_specs=(P(("groups", "dp"), "hidden"), P(("groups", "dp"), "hidden")),
        check_vma=False,
    )
```

```python
import math

import jax
import jax.numpy as jnp
from jax import lax
from jax.sharding import PartitionSpec as P


SEQ = 512
epsilon = 1e-05
HI = lax.Precision.HIGHEST


def exchange(blocks, axis):
    n = lax.axis_size(axis)
    me = lax.axis_index(axis)
    got = [lax.dynamic_index_in_dim(blocks, me, 0, keepdims=False)]
    for d in range(1, n):
        piece = lax.dynamic_index_in_dim(blocks, (me + d) % n, 0, keepdims=False)
        got.append(lax.ppermute(piece, axis, [(i, (i + d) % n) for i in range(n)]))
    return got


def reduce_scatter(blocks, axis):
    got = exchange(blocks, axis)
    acc = got[0]
    for g in got[1:]:
        acc = acc + g
    return acc


def all_gather(x, axis):
    n = lax.axis_size(axis)
    me = lax.axis_index(axis)
    out = jnp.zeros((n,) + x.shape, x.dtype)
    out = lax.dynamic_update_index_in_dim(out, x, me, 0)
    for d in range(1, n):
        got = lax.ppermute(x, axis, [(i, (i + d) % n) for i in range(n)])
        out = lax.dynamic_update_index_in_dim(out, got, (me - d) % n, 0)
    return out


def body(activations, cotangent, up_factor_matrix, input_sketch, rank_sketch):
    shards = lax.axis_size("hidden")
    examples = activations.shape[0] // SEQ
    k_r = rank_sketch.shape[1]
    folded = jnp.dot(up_factor_matrix.astype(jnp.float32), rank_sketch, precision=HI)
    high_f32 = lax.reduce_precision(folded, exponent_bits=8, mantissa_bits=7)
    high = high_f32.astype(jnp.bfloat16)
    low = (folded - high_f32).astype(jnp.bfloat16)
    pad = jnp.zeros((folded.shape[0], max(128 - 2 * k_r, 0)), jnp.bfloat16)
    both = jnp.dot(cotangent, jnp.concatenate([high, low, pad], axis=1),
                   preferred_element_type=jnp.float32)
    rank_t = (both[:, :k_r] + both[:, k_r:2 * k_r]).T
    own_a = rank_t.shape[0] // shards
    rank_own = reduce_scatter(rank_t.reshape(shards, own_a, -1), "hidden")
    input_part = jnp.dot(activations, input_sketch, preferred_element_type=jnp.float32)
    input_rows = input_part.reshape(examples, SEQ, input_part.shape[1])

    def outer(rank_block):
        rows = rank_block.reshape(own_a, examples, SEQ)
        return jnp.einsum("aes,esb->eab", rows, input_rows, precision=HI)

    own = outer(rank_own)
    for d in range(1, shards):
        visiting = lax.ppermute(rank_own, "hidden", [(i, (i + d) % shards) for i in range(shards)])
        back = [(i, (i - d) % shards) for i in range(shards)]
        own = own + lax.ppermute(outer(visiting), "hidden", back)
    features = own.reshape(examples, -1).astype(jnp.bfloat16)
    widened = features.astype(jnp.float32)
    every = all_gather(features, "dp").reshape(-1, features.shape[1]).astype(jnp.float32)
    all_count = every.shape[0]
    weight = 1.0 / (jnp.sum(every * every, axis=0) / all_count + epsilon)
    partial_scores = jnp.dot(widened * weight, every.T, precision=HI)
    feat_total = features.shape[1] * shards
    score_blocks = partial_scores.reshape(examples, shards, -1).transpose(1, 0, 2)
    scores = reduce_scatter(score_blocks, "hidden") / math.sqrt(feat_total)
    return (features, scores)


def solution(mesh):
    placed = (
        P(("groups", "dp"), "hidden"),
        P(("groups", "dp"), "hidden"),
        P("hidden", None),
        P("hidden", None),
        P(),
    )
    return jax.shard_map(
        body,
        mesh=mesh,
        in_specs=placed,
        out_specs=(P(("groups", "dp"), "hidden"), P(("groups", "dp"), "hidden")),
        check_vma=False,
    )
```

```python
import math

import jax
import jax.numpy as jnp
from jax import lax
from jax.sharding import PartitionSpec as P


SEQ = 512
epsilon = 1e-05


def exchange(blocks, axis):
    n = lax.axis_size(axis)
    me = lax.axis_index(axis)
    got = [lax.dynamic_index_in_dim(blocks, me, 0, keepdims=False)]
    for d in range(1, n):
        piece = lax.dynamic_index_in_dim(blocks, (me + d) % n, 0, keepdims=False)
        got.append(lax.ppermute(piece, axis, [(i, (i + d) % n) for i in range(n)]))
    return got


def reduce_scatter(blocks, axis):
    got = exchange(blocks, axis)
    acc = got[0]
    for g in got[1:]:
        acc = acc + g
    return acc


def all_gather(x, axis):
    n = lax.axis_size(axis)
    me = lax.axis_index(axis)
    out = jnp.zeros((n,) + x.shape, x.dtype)
    out = lax.dynamic_update_index_in_dim(out, x, me, 0)
    for d in range(1, n):
        got = lax.ppermute(x, axis, [(i, (i + d) % n) for i in range(n)])
        out = lax.dynamic_update_index_in_dim(out, got, (me - d) % n, 0)
    return out


def body(activations, cotangent, up_factor_matrix, input_sketch, rank_sketch):
    shards = lax.axis_size("hidden")
    examples = activations.shape[0] // SEQ
    backward_t = lax.dot_general(up_factor_matrix, cotangent, (((0,), (1,)), ((), ())),
                                 preferred_element_type=jnp.float32)
    rank_t = lax.dot_general(rank_sketch, backward_t, (((0,), (0,)), ((), ())), precision=lax.Precision.HIGH)
    own_a = rank_t.shape[0] // shards
    rank_own = reduce_scatter(rank_t.reshape(shards, own_a, -1), "hidden")
    input_part = jnp.dot(activations, input_sketch, preferred_element_type=jnp.float32)
    input_rows = input_part.reshape(examples, SEQ, input_part.shape[1])

    def outer(rank_block):
        rows = rank_block.reshape(own_a, examples, SEQ)
        return jnp.einsum("aes,esb->eab", rows, input_rows, precision=lax.Precision.HIGH)

    own = outer(rank_own)
    for d in range(1, shards):
        visiting = lax.ppermute(rank_own, "hidden", [(i, (i + d) % shards) for i in range(shards)])
        back = [(i, (i - d) % shards) for i in range(shards)]
        own = own + lax.ppermute(outer(visiting), "hidden", back)
    features = own.reshape(examples, -1).astype(jnp.bfloat16)
    widened = features.astype(jnp.float32)
    every = all_gather(features, "dp").reshape(-1, features.shape[1]).astype(jnp.float32)
    all_count = every.shape[0]
    weight = 1.0 / (jnp.sum(every * every, axis=0) / all_count + epsilon)
    partial_scores = jnp.dot(widened * weight, every.T, precision=lax.Precision.HIGH)
    feat_total = features.shape[1] * shards
    score_blocks = partial_scores.reshape(examples, shards, -1).transpose(1, 0, 2)
    scores = reduce_scatter(score_blocks, "hidden") / math.sqrt(feat_total)
    return (features, scores)


def solution(mesh):
    placed = (
        P(("groups", "dp"), "hidden"),
        P(("groups", "dp"), "hidden"),
        P("hidden", None),
        P("hidden", None),
        P(),
    )
    return jax.shard_map(
        body,
        mesh=mesh,
        in_specs=placed,
        out_specs=(P(("groups", "dp"), "hidden"), P(("groups", "dp"), "hidden")),
        check_vma=False,
    )
```
